512 devices in a mesh: dp: 32 (over y_hi, z), tensor: 16 (over x, y_lo, core).
Axes of the slice: x: 4, y: 4 (y_hi: 2, y_lo: 2; y = y_hi * 2 + y_lo), z: 16, core: 2. Of those that a mesh axis runs over, the one named last changes fastest.
Arguments:
- residual: bfloat16 [65536, 2048], P(('dp', 'tensor')), may hold values from -0.59765625 to 0.59765625
- queries: bfloat16 [65536, 2048], P(('dp', 'tensor')), may hold values from -27 to 27
- new_keys: bfloat16 [65536, 2048], P(('dp', 'tensor')), may hold values from -27 to 27
- new_values: bfloat16 [65536, 2048], P(('dp', 'tensor')), may hold values from -6 to 6
- lengths: int32 [32, 2], P('dp'), may hold values from 1 to 1536, 2048 in all within a row
- page_order: int32 [32, 17], P('dp'), may hold values from 0 to 16, each once within a row
- wo_shard: float32 [2048, 2048], P('tensor', 'dp'), may hold values from -0.125 to 0.125
- norm_gain: float32 [2048], replicated, may hold values from 0.1 to 1.9
- gate_shard: float32 [16, 2048, 256], P('tensor', 'dp'), may hold values from -0.125 to 0.125
- up_shard: float32 [16, 2048, 256], P('tensor', 'dp'), may hold values from -0.125 to 0.125
- down_shard: float32 [16, 256, 2048], P('tensor', None, 'dp'), may hold values from -0.1875 to 0.1875
- routes: int32 [65536, 8], P(('dp', 'tensor')), may hold values from 0 to 63, as said below
- route_weights: float32 [65536, 8], P(('dp', 'tensor')), may hold values from 0.05 to 0.3
Outputs:
- hidden_mid: bfloat16 [65536, 2048], P(('dp', 'tensor'))
- expert_sum: bfloat16 [65536, 2048], P(('dp', 'tensor'))
- key_pages: bfloat16 [544, 128, 2048], P('dp', None, 'tensor')
- value_pages: bfloat16 [544, 128, 2048], P('dp', None, 'tensor')
The draws below stay inside these ranges and needn't reach their ends.
Inputs may be any that keep to these rules, and one draw needn't show every extreme that they name: `routes`: each row names 8 different experts. Within each aligned block of 128 rows (the rows of one device), each expert below 4 is named by 1 to 16 rows; one of them, the same in all blocks of a draw, by exactly 16 rows in every block, the others by at most 8 rows.
All inputs are finite; a program needn't handle non-finite values.
Results may differ from the reference program's by a relative error of at most 0.015.
Values may be sent and summed in bfloat16 or wider, within the bound.
No kernel may reach another device: no remote copies, remote signals or barrier semaphores. Data moves between devices by JAX's collectives and lax.ppermute only.
A program may use at most 64 MiB of HBM per device.

```python
import math
import jax
import jax.numpy as jnp
import numpy as np
from jax import lax

D = 2048
HEADS = 16
HD = 128
FF = 1024
EXPERTS = 64
TOP = 8
SPLIT = 4
PAGE = 128
REQ_GRP = 2
TOK_DEV = 128
ATT = 2048
PIECE = 256
FLIGHT = 4
TOK_GRP = 2048
TOKENS = 65536
POOL = 17
MOST = 16
N_DP = 32
N_TENSOR = 16


def pair_draw(key):
    base_query = jax.random.normal(jax.random.fold_in(key, 11), (TOKENS, ATT), jnp.float32)
    base_key = jax.random.normal(jax.random.fold_in(key, 12), (TOKENS, ATT), jnp.float32)
    queries_out = 1.5 * jnp.clip(base_query, -6.0, 6.0)
    keys_out = jnp.clip(base_key, -6.0, 6.0)
    return (queries_out, keys_out)


def draw_queries(key, part):
    return pair_draw(key)[0].astype(jnp.bfloat16)


def draw_new_keys(key, part):
    return pair_draw(key)[1].astype(jnp.bfloat16)


def draw_routes(key, part):
    blocks = TOKENS // TOK_DEV
    flight = N_TENSOR // SPLIT
    hottest = jax.random.randint(jax.random.fold_in(key, 21), (), 0, flight)
    counts = jax.random.randint(jax.random.fold_in(key, 22), (blocks, flight), 1, MOST // 2 + 1)
    counts = jnp.where(jnp.arange(flight)[None, :] == hottest, MOST, counts)

    def permute_rows(subkey):
        return jax.random.permutation(subkey, TOK_DEV)
    orders = jax.vmap(permute_rows)(jax.random.split(jax.random.fold_in(key, 23), blocks * flight))
    rank_of = jnp.argsort(orders.reshape(blocks, flight, TOK_DEV), axis=2)
    chosen = rank_of < counts[:, :, None]
    chosen = jnp.transpose(chosen, (0, 2, 1)).reshape(TOKENS, flight)

    def permute_rest(subkey):
        return jax.random.permutation(subkey, EXPERTS - flight)
    others = jax.vmap(permute_rest)(jax.random.split(jax.random.fold_in(key, 24), TOKENS)) + flight
    in_ids = jnp.broadcast_to(jnp.arange(flight)[None, :], (TOKENS, flight))
    all_ids = jnp.concatenate([in_ids, others], axis=1)
    score_in = jnp.where(chosen, in_ids, EXPERTS + in_ids)
    score_rest = jnp.broadcast_to(flight + jnp.arange(EXPERTS - flight)[None, :], (TOKENS, EXPERTS - flight))
    scores = jnp.concatenate([score_in, score_rest], axis=1)
    position = jnp.argsort(scores, axis=1)[:, :TOP]
    picked = jnp.take_along_axis(all_ids, position, axis=1)

    def permute_slots(subkey):
        return jax.random.permutation(subkey, TOP)
    shuffle = jax.vmap(permute_slots)(jax.random.split(jax.random.fold_in(key, 25), TOKENS))
    return jnp.take_along_axis(picked, shuffle, axis=1).astype(jnp.int32)


def levels(rng, extent, cuts, low, top_value):
    factor_of, own = 1.0, jax.random.fold_in(rng, 6)
    for axis_at, parts in cuts:
        steps = jnp.exp(jax.random.uniform(jax.random.fold_in(own, axis_at), (parts,), jnp.float32, low / len(cuts), top_value / len(cuts)))
        factor_of = factor_of * jnp.repeat(steps, extent[axis_at] // parts).reshape([-1 if axis == axis_at else 1 for axis in range(len(extent))])
    return factor_of


def profile(amount, total, most, skew):
    portions = [(1 << 20) // math.isqrt(rank ** skew) + 1 for rank in range(2, amount + 1)]
    surplus, given = total - most - (amount - 1), [1] * (amount - 1)
    while surplus > 0:
        candidates = [i for i in range(amount - 1) if given[i] < most]
        mass, remaining = sum([portions[i] for i in candidates]), surplus
        for i in candidates:
            addition = min(most - given[i], max(1, remaining * portions[i] // mass), surplus)
            given[i] = given[i] + addition
            surplus = surplus - addition
    return np.array([most] + given)


def ragged_sizes(rng, number_of, total, reach, lean):
    if number_of == 2:
        one = jax.random.randint(rng, (), max(1, total - reach), min(reach, total - 1) + 1)
        return jnp.stack([one, total - one])
    tallies = jnp.asarray(profile(number_of, total, reach, lean), jnp.int32)
    couples = (number_of - 1) // 2
    donor, receiver = tallies[1:1 + 2 * couples:2], tallies[2:2 + 2 * couples:2]
    slack = jnp.minimum(donor - 1, reach - receiver)
    moved = jax.random.randint(jax.random.fold_in(rng, 1), (couples,), 0, 1 << 20) % (slack + 1)
    tallies = tallies.at[1:1 + 2 * couples:2].set(donor - moved).at[2:2 + 2 * couples:2].set(receiver + moved)
    return tallies[jax.random.permutation(jax.random.fold_in(rng, 2), number_of)]


def gaussian(stream_key, shape, width, most, shards=(), held_as=jnp.bfloat16):
    entries = width * jax.random.normal(stream_key, shape, jnp.float32)
    if shards:
        entries = entries * levels(stream_key, shape, shards, -0.22, 0.18)
    return jnp.clip(entries, -most, most).astype(held_as)


def setup_inputs(seed: int = 0) -> dict:
    keys = jax.random.split(jax.random.key(seed), 14)
    residual = gaussian(keys[0], (TOKENS, D), 0.1, 0.59765625, ((0, 512),))
    queries = draw_queries(jax.random.fold_in(keys[13], 71), 0)
    new_keys = draw_new_keys(jax.random.fold_in(keys[13], 71), 0)
    new_values = gaussian(keys[3], (TOKENS, ATT), 1.0, 6.0, ((0, 512),))
    lengths = jax.vmap(lambda own: ragged_sizes(own, REQ_GRP, TOK_GRP, TOK_GRP * 3 // 4, 2))(jax.random.split(keys[4], N_DP)).reshape((N_DP, REQ_GRP)).astype(jnp.int32)
    page_order = jax.vmap(lambda own: jax.random.permutation(own, POOL))(jax.random.split(keys[5], N_DP)).reshape((N_DP, POOL)).astype(jnp.int32)
    wo_shard = gaussian(keys[6], (ATT, D), ATT ** -0.5, 0.125, ((0, 16), (1, 32)), jnp.float32)
    norm_gain = jnp.clip(1.0 + 0.18 * jax.random.normal(keys[7], (D,), jnp.float32), 0.1, 1.9)
    gate_shard = gaussian(keys[8], (N_TENSOR, D, PIECE), D ** -0.5, 0.125, ((0, 16), (1, 32)), jnp.float32)
    up_shard = gaussian(keys[9], (N_TENSOR, D, PIECE), D ** -0.5, 0.125, ((0, 16), (1, 32)), jnp.float32)
    down_shard = gaussian(keys[10], (N_TENSOR, PIECE, D), FF ** -0.5, 0.1875, ((0, 16), (2, 32)), jnp.float32)
    routes = draw_routes(jax.random.fold_in(keys[13], 71), 0)
    route_weights = jnp.clip(0.05 + 0.25 * jax.random.uniform(keys[12], (TOKENS, TOP), jnp.float32) ** levels(keys[12], (TOKENS, TOP), ((0, 512),), -0.2, 0.2), 0.05, 0.3)
    return {"residual": residual, "queries": queries, "new_keys": new_keys, "new_values": new_values, "lengths": lengths, "page_order": page_order, "wo_shard": wo_shard, "norm_gain": norm_gain, "gate_shard": gate_shard, "up_shard": up_shard, "down_shard": down_shard, "routes": routes, "route_weights": route_weights}


def page_layout(lens_row, order_row, group_rows, pool_size):
    index_rows = jnp.arange(group_rows, dtype=jnp.int32)
    prompt_ends = jnp.cumsum(lens_row).astype(jnp.int32)
    segment = lax.optimization_barrier(jnp.sum((index_rows[:, None] >= prompt_ends[None, :]).astype(jnp.int32), axis=1))
    prompt_starts = prompt_ends - lens_row
    owner_mask = (segment[:, None] == jnp.arange(lens_row.shape[0], dtype=jnp.int32)[None, :]).astype(jnp.int32)
    begins = lax.optimization_barrier(jnp.sum(owner_mask * prompt_starts[None, :], axis=1))
    page_count = (lens_row + PAGE - 1) // PAGE
    first_page = jnp.cumsum(page_count).astype(jnp.int32) - page_count
    page_first = lax.optimization_barrier(jnp.sum(owner_mask * first_page[None, :], axis=1))
    position = index_rows - begins
    logical = page_first + position // PAGE
    matched = (logical[:, None] == jnp.arange(pool_size, dtype=jnp.int32)[None, :]).astype(jnp.int32)
    physical = lax.optimization_barrier(jnp.sum(matched * order_row[None, :], axis=1))
    return (segment, physical * PAGE + position % PAGE)

def attend_group(q_group, k_group, v_group, segment):
    block_rows = min(512, TOK_GRP)
    count_blocks = TOK_GRP // block_rows
    q_blocks = q_group.reshape(count_blocks, block_rows, HEADS, HD)
    seg_blocks = segment.reshape(count_blocks, block_rows)
    k_float = k_group.reshape(TOK_GRP, HEADS, HD).astype(jnp.float32)
    v_float = v_group.reshape(TOK_GRP, HEADS, HD).astype(jnp.float32)

    def one_block(block_pair):
        q_block, seg_block = block_pair
        scores = jnp.einsum('qhd,khd->hqk', q_block.astype(jnp.float32), k_float) / math.sqrt(HD)
        same_prompt = seg_block[:, None] == segment[None, :]
        scores = jnp.where(same_prompt[None, :, :], scores, -jnp.inf)
        row_max = lax.optimization_barrier(jnp.max(scores, axis=2, keepdims=True))
        weights = jnp.exp(scores - row_max)
        totals = lax.optimization_barrier(jnp.sum(weights, axis=2))
        rounded = lax.optimization_barrier(weights.astype(jnp.bfloat16)).astype(jnp.float32)
        output = jnp.einsum('hqk,khd->qhd', rounded, v_float) / jnp.transpose(totals)[:, :, None]
        return output.astype(jnp.bfloat16).reshape(block_rows, HEADS * HD)
    return lax.map(one_block, (q_blocks, seg_blocks)).reshape(TOK_GRP, HEADS * HD)

def reference(residual, queries, new_keys, new_values, lengths, page_order, wo_shard, norm_gain, gate_shard, up_shard, down_shard, routes, route_weights):

    def per_group(group):
        first_row = (group * TOK_GRP).astype(jnp.int32)
        q_group = lax.dynamic_slice_in_dim(queries, first_row, TOK_GRP, 0)
        k_group = lax.dynamic_slice_in_dim(new_keys, first_row, TOK_GRP, 0)
        v_group = lax.dynamic_slice_in_dim(new_values, first_row, TOK_GRP, 0)
        segment, slot_index = page_layout(lengths[group], page_order[group], TOK_GRP, POOL)
        attended = attend_group(q_group, k_group, v_group, segment)
        key_block = jnp.zeros((POOL * PAGE, ATT), jnp.bfloat16).at[slot_index].set(k_group)
        value_block = jnp.zeros((POOL * PAGE, ATT), jnp.bfloat16).at[slot_index].set(v_group)
        return (attended, key_block, value_block)
    attended, key_block, value_block = lax.map(per_group, jnp.arange(N_DP, dtype=jnp.int32))
    attended = attended.reshape(TOKENS, ATT)
    key_pages = key_block.reshape(N_DP * POOL, PAGE, ATT)
    value_pages = value_block.reshape(N_DP * POOL, PAGE, ATT)
    wo_cast = wo_shard.astype(jnp.bfloat16)
    projected = jnp.dot(attended, wo_cast, preferred_element_type=jnp.float32)
    hidden_mid = (residual.astype(jnp.float32) + projected).astype(jnp.bfloat16)
    mid_float = hidden_mid.astype(jnp.float32)
    normed = (mid_float * lax.rsqrt(lax.optimization_barrier(jnp.mean(mid_float * mid_float, axis=1, keepdims=True)) + 1e-06) * norm_gain).astype(jnp.bfloat16)
    blocks = TOKENS // TOK_DEV
    normed_blocks = normed.reshape(blocks, TOK_DEV, D).astype(jnp.float32)
    route_blocks = routes.reshape(blocks, TOK_DEV, TOP)
    weight_blocks = route_weights.reshape(blocks, TOK_DEV, TOP)
    flight_ids = jnp.arange(FLIGHT, dtype=jnp.int32)
    named_here = route_blocks[:, :, :, None] == flight_ids[None, None, None, :]
    routed = jnp.any(named_here, axis=2)
    weight_sum = lax.optimization_barrier(jnp.sum(jnp.where(named_here, weight_blocks[:, :, :, None], 0.0), axis=2))
    ranked = jnp.cumsum(routed.astype(jnp.int32), axis=1) - 1
    picked = ((ranked[:, :, :, None] == jnp.arange(MOST, dtype=jnp.int32)[None, None, None, :]) & routed[:, :, :, None]).astype(jnp.float32)
    mixing = picked * weight_sum[:, :, :, None]

    def per_expert(expert, running):
        chosen = lax.dynamic_index_in_dim(picked, expert, 2, keepdims=False)
        gathered = jnp.einsum('btm,btd->bmd', chosen, normed_blocks, precision=lax.Precision.HIGHEST)
        expert_rows = gathered.astype(jnp.bfloat16).reshape(blocks * MOST, D)
        summed = jnp.zeros((blocks * MOST, D), jnp.float32)
        for part_index in range(SPLIT):
            piece_index = (expert * SPLIT + part_index).astype(jnp.int32)
            gate_w = lax.dynamic_index_in_dim(gate_shard, piece_index, 0, keepdims=False).astype(jnp.bfloat16)
            up_w = lax.dynamic_index_in_dim(up_shard, piece_index, 0, keepdims=False).astype(jnp.bfloat16)
            down_w = lax.dynamic_index_in_dim(down_shard, piece_index, 0, keepdims=False).astype(jnp.bfloat16)
            gate_val = jnp.dot(expert_rows, gate_w, preferred_element_type=jnp.float32)
            up_val = jnp.dot(expert_rows, up_w, preferred_element_type=jnp.float32)
            inner_act = (jax.nn.silu(gate_val) * up_val).astype(jnp.bfloat16)
            result = jnp.dot(inner_act, down_w, preferred_element_type=jnp.float32).astype(jnp.bfloat16)
            summed = summed + result.astype(jnp.float32)
        weighting = lax.dynamic_index_in_dim(mixing, expert, 2, keepdims=False)
        added = jnp.einsum('btm,bmd->btd', weighting, summed.reshape(blocks, MOST, D), precision=lax.Precision.HIGHEST)
        return running + added
    total_sum = lax.fori_loop(0, FLIGHT, per_expert, jnp.zeros((blocks, TOK_DEV, D), jnp.float32))
    expert_sum = total_sum.reshape(TOKENS, D).astype(jnp.bfloat16)
    return (hidden_mid, expert_sum, key_pages, value_pages)
```

```python
import math

import jax
import jax.numpy as jnp
from jax import lax
from jax.sharding import Mesh, PartitionSpec as P

D = 2048
HEADS = 16
HD = 128
SPLIT = 4
PAGE = 128
MOST = 16


def page_layout(lens_row, order_row, group_rows, pool_size):
    index_rows = jnp.arange(group_rows, dtype=jnp.int32)
    prompt_ends = jnp.cumsum(lens_row)
    segment = jnp.sum((index_rows[:, None] >= prompt_ends[None, :]).astype(jnp.int32), axis=1)
    prompt_starts = prompt_ends - lens_row
    owner_mask = (
        segment[:, None] == jnp.arange(lens_row.shape[0], dtype=jnp.int32)[None, :]
    ).astype(jnp.int32)
    begins = jnp.sum(owner_mask * prompt_starts[None, :], axis=1)
    page_count = (lens_row + PAGE - 1) // PAGE
    first_page = jnp.cumsum(page_count) - page_count
    page_first = jnp.sum(owner_mask * first_page[None, :], axis=1)
    position = index_rows - begins
    logical = page_first + position // PAGE
    matched = (logical[:, None] == jnp.arange(pool_size, dtype=jnp.int32)[None, :]).astype(
        jnp.int32
    )
    physical = jnp.sum(matched * order_row[None, :], axis=1)
    return (segment, physical * PAGE + position % PAGE)


def attend_group(q_heads, k_heads, v_heads, segment, heads_here):
    group_rows = q_heads.shape[0]
    block_rows = min(512, group_rows)
    count_blocks = group_rows // block_rows
    q_blocks = q_heads.reshape(count_blocks, block_rows, heads_here, HD)
    seg_blocks = segment.reshape(count_blocks, block_rows)
    k_split = k_heads.reshape(group_rows, heads_here, HD)
    v_split = v_heads.reshape(group_rows, heads_here, HD)

    def one_block(block_pair):
        q_block, seg_block = block_pair
        scores = jnp.einsum(
            "qhd,khd->hqk", q_block, k_split, preferred_element_type=jnp.float32
        ) / math.sqrt(HD)
        same_prompt = seg_block[:, None] == segment[None, :]
        scores = jnp.where(same_prompt[None, :, :], scores, -jnp.inf)
        row_max = jnp.max(scores, axis=2, keepdims=True)
        weights = jnp.exp(scores - row_max)
        totals = jnp.sum(weights, axis=2)
        output = jnp.einsum(
            "hqk,khd->qhd",
            weights.astype(jnp.bfloat16),
            v_split,
            preferred_element_type=jnp.float32,
        )
        output = output / jnp.transpose(totals)[:, :, None]
        return output.astype(jnp.bfloat16).reshape(block_rows, heads_here * HD)

    return lax.map(one_block, (q_blocks, seg_blocks)).reshape(group_rows, heads_here * HD)


def gather_dp(pieces):
    flat = jnp.concatenate([p.reshape(-1) for p in pieces])
    lanes = 128
    packed = flat.reshape(-1, lanes)
    gathered = lax.all_gather(lax.all_gather(packed, "dh"), "dz")
    gathered = jnp.swapaxes(gathered, 0, 1).reshape(-1, flat.shape[0])
    out, at = [], 0
    for p in pieces:
        out.append(gathered[:, at : at + p.size].reshape((-1,) + p.shape))
        at += p.size
    return out


def body(
    residual,
    queries,
    new_keys,
    new_values,
    lengths,
    page_order,
    wo_shard,
    norm_gain,
    gate_shard,
    up_shard,
    down_shard,
    routes,
    route_weights,
):
    tensor_count = lax.axis_size("tensor")
    heads_here = HEADS // tensor_count
    q_heads, k_heads, v_heads = (
        lax.all_to_all(queries, "tensor", split_axis=1, concat_axis=0, tiled=True),
        lax.all_to_all(new_keys, "tensor", split_axis=1, concat_axis=0, tiled=True),
        lax.all_to_all(new_values, "tensor", split_axis=1, concat_axis=0, tiled=True),
    )
    group_rows = q_heads.shape[0]
    pool_size = page_order.shape[1]
    segment, slot_index = page_layout(lengths[0], page_order[0], group_rows, pool_size)
    head_width = k_heads.shape[1]
    key_pages = (
        jnp.zeros((pool_size * PAGE, head_width), jnp.bfloat16)
        .at[slot_index]
        .set(k_heads)
        .reshape(pool_size, PAGE, head_width)
    )
    value_pages = (
        jnp.zeros((pool_size * PAGE, head_width), jnp.bfloat16)
        .at[slot_index]
        .set(v_heads)
        .reshape(pool_size, PAGE, head_width)
    )
    attended = attend_group(q_heads, k_heads, v_heads, segment, heads_here)
    token_rows = lax.all_to_all(attended, "tensor", split_axis=0, concat_axis=1, tiled=True)
    weights_full = gather_dp(
        [
            wo_shard.astype(jnp.bfloat16),
            gate_shard[0].astype(jnp.bfloat16),
            up_shard[0].astype(jnp.bfloat16),
            down_shard[0].astype(jnp.bfloat16),
        ]
    )
    wo_rows = weights_full[0].transpose(1, 0, 2).reshape(wo_shard.shape[0], -1)
    gate_full = weights_full[1].reshape(1, -1, gate_shard.shape[2])
    up_full = weights_full[2].reshape(1, -1, up_shard.shape[2])
    down_full = weights_full[3].transpose(1, 0, 2).reshape(1, down_shard.shape[1], -1)
    projected = jnp.dot(
        token_rows,
        lax.all_gather(wo_rows, "tensor", axis=0, tiled=True),
        preferred_element_type=jnp.float32,
    )
    hidden_mid = (residual.astype(jnp.float32) + projected).astype(jnp.bfloat16)
    mid_float = hidden_mid.astype(jnp.float32)
    normed = (
        mid_float
        * lax.rsqrt(jnp.mean(mid_float * mid_float, axis=1, keepdims=True) + 1e-06)
        * norm_gain
    ).astype(jnp.bfloat16)
    flight = tensor_count // SPLIT
    flight_ids = jnp.arange(flight, dtype=jnp.int32)
    named_here = routes[:, :, None] == flight_ids[None, None, :]
    routed = jnp.any(named_here, axis=1)
    weight_sum = jnp.sum(jnp.where(named_here, route_weights[:, :, None], 0.0), axis=1)
    ranked = jnp.cumsum(routed.astype(jnp.int32), axis=0) - 1
    picked = (ranked[:, :, None] == jnp.arange(MOST, dtype=jnp.int32)[None, None, :]) & routed[
        :, :, None
    ]
    outgoing = jnp.einsum(
        "tem,td->emd", picked.astype(jnp.bfloat16), normed, preferred_element_type=jnp.float32
    ).astype(jnp.bfloat16)
    outgoing = jnp.repeat(outgoing, SPLIT, axis=0)
    arrived = lax.all_to_all(outgoing, "tensor", split_axis=0, concat_axis=0, tiled=True)
    gate_val = jnp.einsum("smd,dp->smp", arrived, gate_full[0], preferred_element_type=jnp.float32)
    up_val = jnp.einsum("smd,dp->smp", arrived, up_full[0], preferred_element_type=jnp.float32)
    inner_act = (jax.nn.silu(gate_val) * up_val).astype(jnp.bfloat16)
    result = jnp.einsum(
        "smp,pd->smd", inner_act, down_full[0], preferred_element_type=jnp.float32
    ).astype(jnp.bfloat16)
    returned = lax.all_to_all(result, "tensor", split_axis=0, concat_axis=0, tiled=True)
    summed = jnp.sum(returned.reshape(flight, SPLIT, MOST, D).astype(jnp.float32), axis=1)
    mixing = picked.astype(jnp.float32) * weight_sum[:, :, None]
    expert_sum = jnp.einsum("tem,emd->td", mixing, summed, precision=lax.Precision.HIGHEST).astype(
        jnp.bfloat16
    )
    return (hidden_mid, expert_sum, key_pages, value_pages)


def solution(mesh):
    dp_count = mesh.shape["dp"]
    dz_count = 16 if dp_count % 16 == 0 else dp_count
    split_mesh = Mesh(
        mesh.devices.reshape(dp_count // dz_count, dz_count, mesh.shape["tensor"]),
        ("dh", "dz", "tensor"),
    )
    return jax.shard_map(
        body,
        mesh=split_mesh,
        in_specs=(
            P(("dh", "dz", "tensor"), None),
            P(("dh", "dz", "tensor"), None),
            P(("dh", "dz", "tensor"), None),
            P(("dh", "dz", "tensor"), None),
            P(("dh", "dz"), None),
            P(("dh", "dz"), None),
            P("tensor", ("dh", "dz")),
            P(),
            P("tensor", ("dh", "dz"), None),
            P("tensor", ("dh", "dz"), None),
            P("tensor", None, ("dh", "dz")),
            P(("dh", "dz", "tensor"), None),
            P(("dh", "dz", "tensor"), None),
        ),
        out_specs=(
            P(("dh", "dz", "tensor"), None),
            P(("dh", "dz", "tensor"), None),
            P(("dh", "dz"), None, "tensor"),
            P(("dh", "dz"), None, "tensor"),
        ),
        check_vma=False,
    )
```

```python
import math

import jax
import jax.numpy as jnp
from jax import lax
from jax.sharding import Mesh, PartitionSpec as P

D = 2048
HEADS = 16
HD = 128
SPLIT = 4
PAGE = 128
MOST = 16


def page_layout(lens_row, order_row, group_rows, pool_size):
    index_rows = jnp.arange(group_rows, dtype=jnp.int32)
    prompt_ends = jnp.cumsum(lens_row)
    segment = jnp.sum((index_rows[:, None] >= prompt_ends[None, :]).astype(jnp.int32), axis=1)
    prompt_starts = prompt_ends - lens_row
    owner_mask = (
        segment[:, None] == jnp.arange(lens_row.shape[0], dtype=jnp.int32)[None, :]
    ).astype(jnp.int32)
    begins = jnp.sum(owner_mask * prompt_starts[None, :], axis=1)
    page_count = (lens_row + PAGE - 1) // PAGE
    first_page = jnp.cumsum(page_count) - page_count
    page_first = jnp.sum(owner_mask * first_page[None, :], axis=1)
    position = index_rows - begins
    logical = page_first + position // PAGE
    matched = (logical[:, None] == jnp.arange(pool_size, dtype=jnp.int32)[None, :]).astype(
        jnp.int32
    )
    physical = jnp.sum(matched * order_row[None, :], axis=1)
    return (segment, physical * PAGE + position % PAGE)


def attend_group(q_heads, k_heads, v_heads, segment, heads_here):
    group_rows = q_heads.shape[0]
    block_rows = min(512, group_rows)
    count_blocks = group_rows // block_rows
    q_blocks = q_heads.reshape(count_blocks, block_rows, heads_here, HD)
    seg_blocks = segment.reshape(count_blocks, block_rows)
    k_split = k_heads.reshape(group_rows, heads_here, HD)
    v_split = v_heads.reshape(group_rows, heads_here, HD)

    def one_block(block_pair):
        q_block, seg_block = block_pair
        scores = jnp.einsum(
            "qhd,khd->hqk", q_block, k_split, preferred_element_type=jnp.float32
        ) / math.sqrt(HD)
        same_prompt = seg_block[:, None] == segment[None, :]
        scores = jnp.where(same_prompt[None, :, :], scores, -jnp.inf)
        row_max = jnp.max(scores, axis=2, keepdims=True)
        weights = jnp.exp(scores - row_max)
        totals = jnp.sum(weights, axis=2)
        output = jnp.einsum(
            "hqk,khd->qhd",
            weights.astype(jnp.bfloat16),
            v_split,
            preferred_element_type=jnp.float32,
        )
        output = output / jnp.transpose(totals)[:, :, None]
        return output.astype(jnp.bfloat16).reshape(block_rows, heads_here * HD)

    return lax.map(one_block, (q_blocks, seg_blocks)).reshape(group_rows, heads_here * HD)


def gather_dp(pieces):
    flat = jnp.concatenate([p.reshape(-1) for p in pieces])
    lanes = 128
    packed = flat.reshape(-1, lanes)
    gathered = lax.all_gather(lax.all_gather(packed, "dh"), "dz")
    gathered = jnp.swapaxes(gathered, 0, 1).reshape(-1, flat.shape[0])
    out, at = [], 0
    for p in pieces:
        out.append(gathered[:, at : at + p.size].reshape((-1,) + p.shape))
        at += p.size
    return out


def ring_gather(block, axis):
    n = lax.axis_size(axis)
    me = lax.axis_index(axis)
    fwd = [(i, (i + 1) % n) for i in range(n)]
    bwd = [(i, (i - 1) % n) for i in range(n)]
    relative = [None] * n
    relative[0] = block
    a = b = block
    for step in range(n // 2):
        a = lax.ppermute(a, axis, fwd)
        relative[n - 1 - step] = a
        if step + 1 < n - 1 - step:
            b = lax.ppermute(b, axis, bwd)
            relative[step + 1] = b
    stacked = jnp.stack(relative + relative)
    return lax.dynamic_slice_in_dim(stacked, n - me, n, axis=0)


def body(
    residual,
    queries,
    new_keys,
    new_values,
    lengths,
    page_order,
    wo_shard,
    norm_gain,
    gate_shard,
    up_shard,
    down_shard,
    routes,
    route_weights,
):
    tensor_count = lax.axis_size("tensor")
    heads_here = HEADS // tensor_count
    q_heads, k_heads, v_heads = (
        lax.all_to_all(queries, "tensor", split_axis=1, concat_axis=0, tiled=True),
        lax.all_to_all(new_keys, "tensor", split_axis=1, concat_axis=0, tiled=True),
        lax.all_to_all(new_values, "tensor", split_axis=1, concat_axis=0, tiled=True),
    )
    group_rows = q_heads.shape[0]
    pool_size = page_order.shape[1]
    segment, slot_index = page_layout(lengths[0], page_order[0], group_rows, pool_size)
    head_width = k_heads.shape[1]
    key_pages = (
        jnp.zeros((pool_size * PAGE, head_width), jnp.bfloat16)
        .at[slot_index]
        .set(k_heads)
        .reshape(pool_size, PAGE, head_width)
    )
    value_pages = (
        jnp.zeros((pool_size * PAGE, head_width), jnp.bfloat16)
        .at[slot_index]
        .set(v_heads)
        .reshape(pool_size, PAGE, head_width)
    )
    k_heads, v_heads, key_pages, value_pages = lax.optimization_barrier(
        (k_heads, v_heads, key_pages, value_pages)
    )
    attended = attend_group(q_heads, k_heads, v_heads, segment, heads_here)
    token_rows = lax.all_to_all(attended, "tensor", split_axis=0, concat_axis=1, tiled=True)
    wo_full = gather_dp([wo_shard.astype(jnp.bfloat16)])[0]
    wo_rows = wo_full.transpose(1, 0, 2).reshape(wo_shard.shape[0], -1)
    expert_pieces = [
        gate_shard[0].astype(jnp.bfloat16),
        up_shard[0].astype(jnp.bfloat16),
        down_shard[0].astype(jnp.bfloat16),
    ]
    expert_flat = jnp.concatenate([p.reshape(-1) for p in expert_pieces]).reshape(-1, 128)
    expert_pairs = lax.all_gather(expert_flat, "dh")
    expert_all = jnp.swapaxes(ring_gather(expert_pairs, "dz"), 0, 1)
    expert_all = expert_all.reshape(-1, expert_flat.size)
    at = 0
    weights_full = []
    for p in expert_pieces:
        weights_full.append(expert_all[:, at : at + p.size].reshape((-1,) + p.shape))
        at += p.size
    gate_full = weights_full[0].reshape(1, -1, gate_shard.shape[2])
    up_full = weights_full[1].reshape(1, -1, up_shard.shape[2])
    down_full = weights_full[2].transpose(1, 0, 2).reshape(1, down_shard.shape[1], -1)
    projected = jnp.dot(
        token_rows,
        lax.all_gather(wo_rows, "tensor", axis=0, tiled=True),
        preferred_element_type=jnp.float32,
    )
    hidden_mid = (residual.astype(jnp.float32) + projected).astype(jnp.bfloat16)
    mid_float = hidden_mid.astype(jnp.float32)
    normed = (
        mid_float
        * lax.rsqrt(jnp.mean(mid_float * mid_float, axis=1, keepdims=True) + 1e-06)
        * norm_gain
    ).astype(jnp.bfloat16)
    flight = tensor_count // SPLIT
    flight_ids = jnp.arange(flight, dtype=jnp.int32)
    named_here = routes[:, :, None] == flight_ids[None, None, :]
    routed = jnp.any(named_here, axis=1)
    weight_sum = jnp.sum(jnp.where(named_here, route_weights[:, :, None], 0.0), axis=1)
    ranked = jnp.cumsum(routed.astype(jnp.int32), axis=0) - 1
    picked = (ranked[:, :, None] == jnp.arange(MOST, dtype=jnp.int32)[None, None, :]) & routed[
        :, :, None
    ]
    outgoing = jnp.einsum(
        "tem,td->emd", picked.astype(jnp.bfloat16), normed, preferred_element_type=jnp.float32
    ).astype(jnp.bfloat16)
    outgoing = jnp.repeat(outgoing, SPLIT, axis=0)
    arrived = lax.all_to_all(outgoing, "tensor", split_axis=0, concat_axis=0, tiled=True)
    gate_val = jnp.einsum("smd,dp->smp", arrived, gate_full[0], preferred_element_type=jnp.float32)
    up_val = jnp.einsum("smd,dp->smp", arrived, up_full[0], preferred_element_type=jnp.float32)
    inner_act = (jax.nn.silu(gate_val) * up_val).astype(jnp.bfloat16)
    result = jnp.einsum(
        "smp,pd->smd", inner_act, down_full[0], preferred_element_type=jnp.float32
    ).astype(jnp.bfloat16)
    returned = lax.all_to_all(result, "tensor", split_axis=0, concat_axis=0, tiled=True)
    summed = jnp.sum(returned.reshape(flight, SPLIT, MOST, D).astype(jnp.float32), axis=1)
    mixing = picked.astype(jnp.float32) * weight_sum[:, :, None]
    expert_sum = jnp.einsum("tem,emd->td", mixing, summed, precision=lax.Precision.HIGHEST).astype(
        jnp.bfloat16
    )
    return (hidden_mid, expert_sum, key_pages, value_pages)


def solution(mesh):
    dp_count = mesh.shape["dp"]
    dz_count = 16 if dp_count % 16 == 0 else dp_count
    split_mesh = Mesh(
        mesh.devices.reshape(dp_count // dz_count, dz_count, mesh.shape["tensor"]),
        ("dh", "dz", "tensor"),
    )
    return jax.shard_map(
        body,
        mesh=split_mesh,
        in_specs=(
            P(("dh", "dz", "tensor"), None),
            P(("dh", "dz", "tensor"), None),
            P(("dh", "dz", "tensor"), None),
            P(("dh", "dz", "tensor"), None),
            P(("dh", "dz"), None),
            P(("dh", "dz"), None),
            P("tensor", ("dh", "dz")),
            P(),
            P("tensor", ("dh", "dz"), None),
            P("tensor", ("dh", "dz"), None),
            P("tensor", None, ("dh", "dz")),
            P(("dh", "dz", "tensor"), None),
            P(("dh", "dz", "tensor"), None),
        ),
        out_specs=(
            P(("dh", "dz", "tensor"), None),
            P(("dh", "dz", "tensor"), None),
            P(("dh", "dz"), None, "tensor"),
            P(("dh", "dz"), None, "tensor"),
        ),
        check_vma=False,
    )
```

```python
import math

import jax
import jax.numpy as jnp
from jax import lax
from jax.sharding import Mesh, PartitionSpec as P

D = 2048
HEADS = 16
HD = 128
SPLIT = 4
PAGE = 128
MOST = 16


def page_layout(lens_row, order_row, group_rows, pool_size):
    index_rows = jnp.arange(group_rows, dtype=jnp.int32)
    prompt_ends = jnp.cumsum(lens_row)
    segment = jnp.sum((index_rows[:, None] >= prompt_ends[None, :]).astype(jnp.int32), axis=1)
    prompt_starts = prompt_ends - lens_row
    owner_mask = (
        segment[:, None] == jnp.arange(lens_row.shape[0], dtype=jnp.int32)[None, :]
    ).astype(jnp.int32)
    begins = jnp.sum(owner_mask * prompt_starts[None, :], axis=1)
    page_count = (lens_row + PAGE - 1) // PAGE
    first_page = jnp.cumsum(page_count) - page_count
    page_first = jnp.sum(owner_mask * first_page[None, :], axis=1)
    position = index_rows - begins
    logical = page_first + position // PAGE
    matched = (logical[:, None] == jnp.arange(pool_size, dtype=jnp.int32)[None, :]).astype(
        jnp.int32
    )
    physical = jnp.sum(matched * order_row[None, :], axis=1)
    return (segment, physical * PAGE + position % PAGE)


def attend_group(q_heads, k_heads, v_heads, segment, heads_here):
    group_rows = q_heads.shape[0]
    block_rows = min(512, group_rows)
    count_blocks = group_rows // block_rows
    q_blocks = q_heads.reshape(count_blocks, block_rows, heads_here, HD)
    seg_blocks = segment.reshape(count_blocks, block_rows)
    k_split = k_heads.reshape(group_rows, heads_here, HD)
    v_split = v_heads.reshape(group_rows, heads_here, HD)

    def one_block(block_pair):
        q_block, seg_block = block_pair
        scores = jnp.einsum(
            "qhd,khd->hqk", q_block, k_split, preferred_element_type=jnp.float32
        ) / math.sqrt(HD)
        same_prompt = seg_block[:, None] == segment[None, :]
        scores = jnp.where(same_prompt[None, :, :], scores, -jnp.inf)
        row_max = jnp.max(scores, axis=2, keepdims=True)
        weights = jnp.exp(scores - row_max)
        totals = jnp.sum(weights, axis=2)
        output = jnp.einsum(
            "hqk,khd->qhd",
            weights.astype(jnp.bfloat16),
            v_split,
            preferred_element_type=jnp.float32,
        )
        output = output / jnp.transpose(totals)[:, :, None]
        return output.astype(jnp.bfloat16).reshape(block_rows, heads_here * HD)

    return lax.map(one_block, (q_blocks, seg_blocks)).reshape(group_rows, heads_here * HD)


def body(
    residual,
    queries,
    new_keys,
    new_values,
    lengths,
    page_order,
    wo_shard,
    norm_gain,
    gate_shard,
    up_shard,
    down_shard,
    routes,
    route_weights,
):
    tensor_count = lax.axis_size("tensor")
    heads_here = HEADS // tensor_count
    q_heads, k_heads, v_heads = (
        lax.all_to_all(queries, "tensor", split_axis=1, concat_axis=0, tiled=True),
        lax.all_to_all(new_keys, "tensor", split_axis=1, concat_axis=0, tiled=True),
        lax.all_to_all(new_values, "tensor", split_axis=1, concat_axis=0, tiled=True),
    )
    group_rows = q_heads.shape[0]
    pool_size = page_order.shape[1]
    segment, slot_index = page_layout(lengths[0], page_order[0], group_rows, pool_size)
    head_width = k_heads.shape[1]
    key_pages = (
        jnp.zeros((pool_size * PAGE, head_width), jnp.bfloat16)
        .at[slot_index]
        .set(k_heads)
        .reshape(pool_size, PAGE, head_width)
    )
    value_pages = (
        jnp.zeros((pool_size * PAGE, head_width), jnp.bfloat16)
        .at[slot_index]
        .set(v_heads)
        .reshape(pool_size, PAGE, head_width)
    )
    pieces = [
        wo_shard.astype(jnp.bfloat16).T,
        gate_shard[0].astype(jnp.bfloat16),
        up_shard[0].astype(jnp.bfloat16),
        down_shard[0].astype(jnp.bfloat16),
    ]
    packed = jnp.concatenate([p.reshape(-1) for p in pieces]).reshape(-1, 128)
    gathered = lax.all_gather(lax.all_gather(packed, "dh"), "dz")
    gathered, q_heads, k_heads, v_heads, key_pages, value_pages = lax.optimization_barrier(
        (gathered, q_heads, k_heads, v_heads, key_pages, value_pages)
    )
    wo_piece_rows = pieces[0].size // 128
    wo_cols = jnp.swapaxes(gathered[:, :, :wo_piece_rows], 0, 1).reshape(-1, pieces[0].shape[1])
    wo_full = lax.all_gather(wo_cols, "tensor", axis=1, tiled=True)
    experts = jnp.swapaxes(gathered[:, :, wo_piece_rows:], 0, 1)
    experts = experts.reshape(experts.shape[0] * experts.shape[1], -1)
    weights_full, at = [], 0
    for p in pieces[1:]:
        weights_full.append(experts[:, at : at + p.size].reshape((-1,) + p.shape))
        at += p.size
    gate_full = weights_full[0].reshape(1, -1, gate_shard.shape[2])
    up_full = weights_full[1].reshape(1, -1, up_shard.shape[2])
    down_full = weights_full[2].transpose(1, 0, 2).reshape(1, down_shard.shape[1], -1)
    attended = attend_group(q_heads, k_heads, v_heads, segment, heads_here)
    token_rows = lax.all_to_all(attended, "tensor", split_axis=0, concat_axis=1, tiled=True)
    projected = jnp.einsum("tr,cr->tc", token_rows, wo_full, preferred_element_type=jnp.float32)
    hidden_mid = (residual.astype(jnp.float32) + projected).astype(jnp.bfloat16)
    mid_float = hidden_mid.astype(jnp.float32)
    normed = (
        mid_float
        * lax.rsqrt(jnp.mean(mid_float * mid_float, axis=1, keepdims=True) + 1e-06)
        * norm_gain
    ).astype(jnp.bfloat16)
    flight = tensor_count // SPLIT
    flight_ids = jnp.arange(flight, dtype=jnp.int32)
    named_here = routes[:, :, None] == flight_ids[None, None, :]
    routed = jnp.any(named_here, axis=1)
    weight_sum = jnp.sum(jnp.where(named_here, route_weights[:, :, None], 0.0), axis=1)
    ranked = jnp.cumsum(routed.astype(jnp.int32), axis=0) - 1
    picked = (ranked[:, :, None] == jnp.arange(MOST, dtype=jnp.int32)[None, None, :]) & routed[
        :, :, None
    ]
    outgoing = jnp.einsum(
        "tem,td->emd", picked.astype(jnp.bfloat16), normed, preferred_element_type=jnp.float32
    ).astype(jnp.bfloat16)
    outgoing = jnp.repeat(outgoing, SPLIT, axis=0)
    arrived = lax.all_to_all(outgoing, "tensor", split_axis=0, concat_axis=0, tiled=True)
    gate_val = jnp.einsum("smd,dp->smp", arrived, gate_full[0], preferred_element_type=jnp.float32)
    up_val = jnp.einsum("smd,dp->smp", arrived, up_full[0], preferred_element_type=jnp.float32)
    inner_act = (jax.nn.silu(gate_val) * up_val).astype(jnp.bfloat16)
    result = jnp.einsum(
        "smp,pd->smd", inner_act, down_full[0], preferred_element_type=jnp.float32
    ).astype(jnp.bfloat16)
    returned = lax.all_to_all(result, "tensor", split_axis=0, concat_axis=0, tiled=True)
    summed = jnp.sum(returned.reshape(flight, SPLIT, MOST, D).astype(jnp.float32), axis=1)
    mixing = picked.astype(jnp.float32) * weight_sum[:, :, None]
    expert_sum = jnp.einsum("tem,emd->td", mixing, summed, precision=lax.Precision.HIGHEST).astype(
        jnp.bfloat16
    )
    return (hidden_mid, expert_sum, key_pages, value_pages)


def solution(mesh):
    dp_count = mesh.shape["dp"]
    dz_count = 16 if dp_count % 16 == 0 else dp_count
    split_mesh = Mesh(
        mesh.devices.reshape(dp_count // dz_count, dz_count, mesh.shape["tensor"]),
        ("dh", "dz", "tensor"),
    )
    return jax.shard_map(
        body,
        mesh=split_mesh,
        in_specs=(
            P(("dh", "dz", "tensor"), None),
            P(("dh", "dz", "tensor"), None),
            P(("dh", "dz", "tensor"), None),
            P(("dh", "dz", "tensor"), None),
            P(("dh", "dz"), None),
            P(("dh", "dz"), None),
            P("tensor", ("dh", "dz")),
            P(),
            P("tensor", ("dh", "dz"), None),
            P("tensor", ("dh", "dz"), None),
            P("tensor", None, ("dh", "dz")),
            P(("dh", "dz", "tensor"), None),
            P(("dh", "dz", "tensor"), None),
        ),
        out_specs=(
            P(("dh", "dz", "tensor"), None),
            P(("dh", "dz", "tensor"), None),
            P(("dh", "dz"), None, "tensor"),
            P(("dh", "dz"), None, "tensor"),
        ),
        check_vma=False,
    )
```

```python
import math

import jax
import jax.numpy as jnp
from jax import lax
from jax.sharding import Mesh, PartitionSpec as P

D = 2048
HEADS = 16
HD = 128
SPLIT = 4
PAGE = 128
MOST = 16


def page_layout(lens_row, order_row, group_rows, pool_size):
    index_rows = jnp.arange(group_rows, dtype=jnp.int32)
    prompt_ends = jnp.cumsum(lens_row)
    segment = jnp.sum((index_rows[:, None] >= prompt_ends[None, :]).astype(jnp.int32), axis=1)
    prompt_starts = prompt_ends - lens_row
    owner_mask = (
        segment[:, None] == jnp.arange(lens_row.shape[0], dtype=jnp.int32)[None, :]
    ).astype(jnp.int32)
    begins = jnp.sum(owner_mask * prompt_starts[None, :], axis=1)
    page_count = (lens_row + PAGE - 1) // PAGE
    first_page = jnp.cumsum(page_count) - page_count
    page_first = jnp.sum(owner_mask * first_page[None, :], axis=1)
    position = index_rows - begins
    logical = page_first + position // PAGE
    matched = (logical[:, None] == jnp.arange(pool_size, dtype=jnp.int32)[None, :]).astype(
        jnp.int32
    )
    physical = jnp.sum(matched * order_row[None, :], axis=1)
    return (segment, physical * PAGE + position % PAGE)


def attend_group(q_heads, k_heads, v_heads, segment, heads_here):
    group_rows = q_heads.shape[0]
    block_rows = min(512, group_rows)
    count_blocks = group_rows // block_rows
    q_blocks = q_heads.reshape(count_blocks, block_rows, heads_here, HD)
    seg_blocks = segment.reshape(count_blocks, block_rows)
    k_split = k_heads.reshape(group_rows, heads_here, HD)
    v_split = v_heads.reshape(group_rows, heads_here, HD)

    def one_block(block_pair):
        q_block, seg_block = block_pair
        scores = jnp.einsum(
            "qhd,khd->hqk", q_block, k_split, preferred_element_type=jnp.float32
        ) / math.sqrt(HD)
        same_prompt = seg_block[:, None] == segment[None, :]
        scores = jnp.where(same_prompt[None, :, :], scores, -jnp.inf)
        row_max = jnp.max(scores, axis=2, keepdims=True)
        weights = jnp.exp(scores - row_max)
        totals = jnp.sum(weights, axis=2)
        output = jnp.einsum(
            "hqk,khd->qhd",
            weights.astype(jnp.bfloat16),
            v_split,
            preferred_element_type=jnp.float32,
        )
        output = output / jnp.transpose(totals)[:, :, None]
        return output.astype(jnp.bfloat16).reshape(block_rows, heads_here * HD)

    return lax.map(one_block, (q_blocks, seg_blocks)).reshape(group_rows, heads_here * HD)


def body(
    residual,
    queries,
    new_keys,
    new_values,
    lengths,
    page_order,
    wo_shard,
    norm_gain,
    gate_shard,
    up_shard,
    down_shard,
    routes,
    route_weights,
):
    tensor_count = lax.axis_size("tensor")
    heads_here = HEADS // tensor_count
    q_heads, k_heads, v_heads = (
        lax.all_to_all(queries, "tensor", split_axis=1, concat_axis=0, tiled=True),
        lax.all_to_all(new_keys, "tensor", split_axis=1, concat_axis=0, tiled=True),
        lax.all_to_all(new_values, "tensor", split_axis=1, concat_axis=0, tiled=True),
    )
    group_rows = q_heads.shape[0]
    pool_size = page_order.shape[1]
    segment, slot_index = page_layout(lengths[0], page_order[0], group_rows, pool_size)
    head_width = k_heads.shape[1]
    key_pages = (
        jnp.zeros((pool_size * PAGE, head_width), jnp.bfloat16)
        .at[slot_index]
        .set(k_heads)
        .reshape(pool_size, PAGE, head_width)
    )
    value_pages = (
        jnp.zeros((pool_size * PAGE, head_width), jnp.bfloat16)
        .at[slot_index]
        .set(v_heads)
        .reshape(pool_size, PAGE, head_width)
    )
    pieces = [wo_shard.T, gate_shard[0], up_shard[0], down_shard[0]]
    packed = jnp.concatenate([p.reshape(-1) for p in pieces]).astype(jnp.bfloat16).reshape(-1, 128)
    gathered = lax.all_gather(lax.all_gather(packed, "dh"), "dz")
    gathered, q_heads, k_heads, v_heads, key_pages, value_pages = lax.optimization_barrier(
        (gathered, q_heads, k_heads, v_heads, key_pages, value_pages)
    )
    wo_piece_rows = pieces[0].size // 128
    wo_cols = jnp.swapaxes(gathered[:, :, :wo_piece_rows], 0, 1).reshape(-1, pieces[0].shape[1])
    wo_full = lax.all_gather(wo_cols, "tensor", axis=1, tiled=True)
    experts = jnp.swapaxes(gathered[:, :, wo_piece_rows:], 0, 1)
    experts = experts.reshape(experts.shape[0] * experts.shape[1], -1)
    weights_full, at = [], 0
    for p in pieces[1:]:
        weights_full.append(experts[:, at : at + p.size].reshape((-1,) + p.shape))
        at += p.size
    gate_full = weights_full[0].reshape(1, -1, gate_shard.shape[2])
    up_full = weights_full[1].reshape(1, -1, up_shard.shape[2])
    down_full = weights_full[2].transpose(1, 0, 2).reshape(1, down_shard.shape[1], -1)
    attended = attend_group(q_heads, k_heads, v_heads, segment, heads_here)
    attended, gate_full, up_full, down_full = lax.optimization_barrier(
        (attended, gate_full, up_full, down_full)
    )
    token_rows = lax.all_to_all(attended, "tensor", split_axis=0, concat_axis=1, tiled=True)
    projected = jnp.einsum("tr,cr->tc", token_rows, wo_full, preferred_element_type=jnp.float32)
    hidden_mid = (residual.astype(jnp.float32) + projected).astype(jnp.bfloat16)
    mid_float = hidden_mid.astype(jnp.float32)
    normed = (
        mid_float
        * lax.rsqrt(jnp.mean(mid_float * mid_float, axis=1, keepdims=True) + 1e-06)
        * norm_gain
    ).astype(jnp.bfloat16)
    flight = tensor_count // SPLIT
    flight_ids = jnp.arange(flight, dtype=jnp.int32)
    named_here = routes[:, :, None] == flight_ids[None, None, :]
    routed = jnp.any(named_here, axis=1)
    weight_sum = jnp.sum(jnp.where(named_here, route_weights[:, :, None], 0.0), axis=1)
    ranked = jnp.cumsum(routed.astype(jnp.int32), axis=0) - 1
    picked = (ranked[:, :, None] == jnp.arange(MOST, dtype=jnp.int32)[None, None, :]) & routed[
        :, :, None
    ]
    outgoing = jnp.einsum(
        "tem,td->emd", picked.astype(jnp.bfloat16), normed, preferred_element_type=jnp.float32
    ).astype(jnp.bfloat16)
    outgoing = jnp.repeat(outgoing, SPLIT, axis=0)
    arrived = lax.all_to_all(outgoing, "tensor", split_axis=0, concat_axis=0, tiled=True)
    gate_val = jnp.einsum("smd,dp->smp", arrived, gate_full[0], preferred_element_type=jnp.float32)
    up_val = jnp.einsum("smd,dp->smp", arrived, up_full[0], preferred_element_type=jnp.float32)
    inner_act = (jax.nn.silu(gate_val) * up_val).astype(jnp.bfloat16)
    result = jnp.einsum(
        "smp,pd->smd", inner_act, down_full[0], preferred_element_type=jnp.float32
    ).astype(jnp.bfloat16)
    returned = lax.all_to_all(result, "tensor", split_axis=0, concat_axis=0, tiled=True)
    summed = jnp.sum(returned.reshape(flight, SPLIT, MOST, D).astype(jnp.float32), axis=1)
    mixing = picked.astype(jnp.float32) * weight_sum[:, :, None]
    expert_sum = jnp.einsum("tem,emd->td", mixing, summed, precision=lax.Precision.HIGHEST).astype(
        jnp.bfloat16
    )
    return (hidden_mid, expert_sum, key_pages, value_pages)


def solution(mesh):
    dp_count = mesh.shape["dp"]
    dz_count = 16 if dp_count % 16 == 0 else dp_count
    split_mesh = Mesh(
        mesh.devices.reshape(dp_count // dz_count, dz_count, mesh.shape["tensor"]),
        ("dh", "dz", "tensor"),
    )
    return jax.shard_map(
        body,
        mesh=split_mesh,
        in_specs=(
            P(("dh", "dz", "tensor"), None),
            P(("dh", "dz", "tensor"), None),
            P(("dh", "dz", "tensor"), None),
            P(("dh", "dz", "tensor"), None),
            P(("dh", "dz"), None),
            P(("dh", "dz"), None),
            P("tensor", ("dh", "dz")),
            P(),
            P("tensor", ("dh", "dz"), None),
            P("tensor", ("dh", "dz"), None),
            P("tensor", None, ("dh", "dz")),
            P(("dh", "dz", "tensor"), None),
            P(("dh", "dz", "tensor"), None),
        ),
        out_specs=(
            P(("dh", "dz", "tensor"), None),
            P(("dh", "dz", "tensor"), None),
            P(("dh", "dz"), None, "tensor"),
            P(("dh", "dz"), None, "tensor"),
        ),
        check_vma=False,
    )
```

```python
import math

import jax
import jax.numpy as jnp
from jax import lax
from jax.sharding import Mesh, PartitionSpec as P

D = 2048
HEADS = 16
HD = 128
SPLIT = 4
PAGE = 128
MOST = 16


def page_layout(lens_row, order_row, group_rows, pool_size):
    index_rows = jnp.arange(group_rows, dtype=jnp.int32)
    prompt_ends = jnp.cumsum(lens_row)
    segment = jnp.sum((index_rows[:, None] >= prompt_ends[None, :]).astype(jnp.int32), axis=1)
    prompt_starts = prompt_ends - lens_row
    owner_mask = (
        segment[:, None] == jnp.arange(lens_row.shape[0], dtype=jnp.int32)[None, :]
    ).astype(jnp.int32)
    begins = jnp.sum(owner_mask * prompt_starts[None, :], axis=1)
    page_count = (lens_row + PAGE - 1) // PAGE
    first_page = jnp.cumsum(page_count) - page_count
    page_first = jnp.sum(owner_mask * first_page[None, :], axis=1)
    position = index_rows - begins
    logical = page_first + position // PAGE
    matched = (logical[:, None] == jnp.arange(pool_size, dtype=jnp.int32)[None, :]).astype(
        jnp.int32
    )
    physical = jnp.sum(matched * order_row[None, :], axis=1)
    return (segment, physical * PAGE + position % PAGE)


def attend_group(q_heads, k_heads, v_heads, segment, heads_here):
    group_rows = q_heads.shape[0]
    block_rows = min(512, group_rows)
    count_blocks = group_rows // block_rows
    q_blocks = q_heads.reshape(count_blocks, block_rows, heads_here, HD)
    seg_blocks = segment.reshape(count_blocks, block_rows)
    k_split = k_heads.reshape(group_rows, heads_here, HD)
    v_split = v_heads.reshape(group_rows, heads_here, HD)

    def one_block(block_pair):
        q_block, seg_block = block_pair
        scores = jnp.einsum(
            "qhd,khd->hqk", q_block, k_split, preferred_element_type=jnp.float32
        ) / math.sqrt(HD)
        same_prompt = seg_block[:, None] == segment[None, :]
        scores = jnp.where(same_prompt[None, :, :], scores, -jnp.inf)
        row_max = jnp.max(scores, axis=2, keepdims=True)
        weights = jnp.exp(scores - row_max)
        totals = jnp.sum(weights, axis=2)
        output = jnp.einsum(
            "hqk,khd->qhd",
            weights.astype(jnp.bfloat16),
            v_split,
            preferred_element_type=jnp.float32,
        )
        output = output / jnp.transpose(totals)[:, :, None]
        return output.astype(jnp.bfloat16).reshape(block_rows, heads_here * HD)

    return lax.map(one_block, (q_blocks, seg_blocks)).reshape(group_rows, heads_here * HD)


def body(
    residual,
    queries,
    new_keys,
    new_values,
    lengths,
    page_order,
    wo_shard,
    norm_gain,
    gate_shard,
    up_shard,
    down_shard,
    routes,
    route_weights,
):
    tensor_count = lax.axis_size("tensor")
    heads_here = HEADS // tensor_count
    q_heads, k_heads, v_heads = (
        lax.all_to_all(queries, "tensor", split_axis=1, concat_axis=0, tiled=True),
        lax.all_to_all(new_keys, "tensor", split_axis=1, concat_axis=0, tiled=True),
        lax.all_to_all(new_values, "tensor", split_axis=1, concat_axis=0, tiled=True),
    )
    group_rows = q_heads.shape[0]
    pool_size = page_order.shape[1]
    segment, slot_index = page_layout(lengths[0], page_order[0], group_rows, pool_size)
    head_width = k_heads.shape[1]
    key_pages = (
        jnp.zeros((pool_size * PAGE, head_width), jnp.bfloat16)
        .at[slot_index]
        .set(k_heads)
        .reshape(pool_size, PAGE, head_width)
    )
    value_pages = (
        jnp.zeros((pool_size * PAGE, head_width), jnp.bfloat16)
        .at[slot_index]
        .set(v_heads)
        .reshape(pool_size, PAGE, head_width)
    )
    pieces = [wo_shard.T, gate_shard[0], up_shard[0], down_shard[0]]
    packed = jnp.concatenate([p.reshape(-1) for p in pieces]).astype(jnp.bfloat16).reshape(-1, 128)
    gathered = lax.all_gather(lax.all_gather(packed, "dh"), "dz")
    attended = attend_group(q_heads, k_heads, v_heads, segment, heads_here)
    token_rows = lax.all_to_all(attended, "tensor", split_axis=0, concat_axis=1, tiled=True)
    gathered, token_rows, key_pages, value_pages = lax.optimization_barrier(
        (gathered, token_rows, key_pages, value_pages)
    )
    wo_piece_rows = pieces[0].size // 128
    wo_cols = jnp.swapaxes(gathered[:, :, :wo_piece_rows], 0, 1).reshape(-1, pieces[0].shape[1])
    wo_full = lax.all_gather(wo_cols, "tensor", axis=1, tiled=True)
    experts = jnp.swapaxes(gathered[:, :, wo_piece_rows:], 0, 1)
    experts = experts.reshape(experts.shape[0] * experts.shape[1], -1)
    weights_full, at = [], 0
    for p in pieces[1:]:
        weights_full.append(experts[:, at : at + p.size].reshape((-1,) + p.shape))
        at += p.size
    gate_full = weights_full[0].reshape(-1, gate_shard.shape[2])
    up_full = weights_full[1].reshape(-1, up_shard.shape[2])
    down_full = weights_full[2].transpose(1, 0, 2).reshape(down_shard.shape[1], -1)

    flight = tensor_count // SPLIT
    flight_ids = jnp.arange(flight, dtype=jnp.int32)
    named_here = routes[:, :, None] == flight_ids[None, None, :]
    routed = jnp.any(named_here, axis=1)
    weight_sum = jnp.sum(jnp.where(named_here, route_weights[:, :, None], 0.0), axis=1)
    ranked = jnp.cumsum(routed.astype(jnp.int32), axis=0) - 1
    picked = (ranked[:, :, None] == jnp.arange(MOST, dtype=jnp.int32)[None, None, :]) & routed[
        :, :, None
    ]
    selector = picked.astype(jnp.bfloat16)
    outgoing = jnp.concatenate(
        [
            jnp.einsum("tem,td->emd", selector, token_rows, preferred_element_type=jnp.float32),
            jnp.einsum("tem,td->emd", selector, residual, preferred_element_type=jnp.float32),
        ],
        axis=2,
    ).astype(jnp.bfloat16)
    outgoing = jnp.repeat(outgoing, SPLIT, axis=0)
    outgoing, gate_full, up_full, down_full = lax.optimization_barrier(
        (outgoing, gate_full, up_full, down_full)
    )
    arrived = lax.all_to_all(outgoing, "tensor", split_axis=0, concat_axis=0, tiled=True)

    def project_norm(rows_att, rows_res):
        projected = jnp.einsum(
            "...r,cr->...c", rows_att, wo_full, preferred_element_type=jnp.float32
        )
        mid = (rows_res.astype(jnp.float32) + projected).astype(jnp.bfloat16)
        mid_float = mid.astype(jnp.float32)
        normed = (
            mid_float
            * lax.rsqrt(jnp.mean(mid_float * mid_float, axis=-1, keepdims=True) + 1e-06)
            * norm_gain
        ).astype(jnp.bfloat16)
        return mid, normed

    _, arrived_normed = project_norm(arrived[:, :, :D], arrived[:, :, D:])
    gate_val = jnp.einsum("smd,dp->smp", arrived_normed, gate_full, preferred_element_type=jnp.float32)
    up_val = jnp.einsum("smd,dp->smp", arrived_normed, up_full, preferred_element_type=jnp.float32)
    inner_act = (jax.nn.silu(gate_val) * up_val).astype(jnp.bfloat16)
    result = jnp.einsum(
        "smp,pd->smd", inner_act, down_full, preferred_element_type=jnp.float32
    ).astype(jnp.bfloat16)
    returned = lax.all_to_all(result, "tensor", split_axis=0, concat_axis=0, tiled=True)
    hidden_mid, _ = project_norm(token_rows, residual)
    summed = jnp.sum(returned.reshape(flight, SPLIT, MOST, D).astype(jnp.float32), axis=1)
    mixing = picked.astype(jnp.float32) * weight_sum[:, :, None]
    expert_sum = jnp.einsum("tem,emd->td", mixing, summed, precision=lax.Precision.HIGHEST).astype(
        jnp.bfloat16
    )
    return (hidden_mid, expert_sum, key_pages, value_pages)


def solution(mesh):
    dp_count = mesh.shape["dp"]
    dz_count = 16 if dp_count % 16 == 0 else dp_count
    split_mesh = Mesh(
        mesh.devices.reshape(dp_count // dz_count, dz_count, mesh.shape["tensor"]),
        ("dh", "dz", "tensor"),
    )
    return jax.shard_map(
        body,
        mesh=split_mesh,
        in_specs=(
            P(("dh", "dz", "tensor"), None),
            P(("dh", "dz", "tensor"), None),
            P(("dh", "dz", "tensor"), None),
            P(("dh", "dz", "tensor"), None),
            P(("dh", "dz"), None),
            P(("dh", "dz"), None),
            P("tensor", ("dh", "dz")),
            P(),
            P("tensor", ("dh", "dz"), None),
            P("tensor", ("dh", "dz"), None),
            P("tensor", None, ("dh", "dz")),
            P(("dh", "dz", "tensor"), None),
            P(("dh", "dz", "tensor"), None),
        ),
        out_specs=(
            P(("dh", "dz", "tensor"), None),
            P(("dh", "dz", "tensor"), None),
            P(("dh", "dz"), None, "tensor"),
            P(("dh", "dz"), None, "tensor"),
        ),
        check_vma=False,
    )
```

```python
import math

import jax
import jax.numpy as jnp
from jax import lax
from jax.sharding import Mesh, PartitionSpec as P

D = 2048
HEADS = 16
HD = 128
SPLIT = 4
PAGE = 128
MOST = 16


def page_layout(lens_row, order_row, group_rows, pool_size):
    index_rows = jnp.arange(group_rows, dtype=jnp.int32)
    prompt_ends = jnp.cumsum(lens_row)
    segment = jnp.sum((index_rows[:, None] >= prompt_ends[None, :]).astype(jnp.int32), axis=1)
    prompt_starts = prompt_ends - lens_row
    owner_mask = (
        segment[:, None] == jnp.arange(lens_row.shape[0], dtype=jnp.int32)[None, :]
    ).astype(jnp.int32)
    begins = jnp.sum(owner_mask * prompt_starts[None, :], axis=1)
    page_count = (lens_row + PAGE - 1) // PAGE
    first_page = jnp.cumsum(page_count) - page_count
    page_first = jnp.sum(owner_mask * first_page[None, :], axis=1)
    position = index_rows - begins
    logical = page_first + position // PAGE
    matched = (logical[:, None] == jnp.arange(pool_size, dtype=jnp.int32)[None, :]).astype(
        jnp.int32
    )
    physical = jnp.sum(matched * order_row[None, :], axis=1)
    return (segment, physical * PAGE + position % PAGE)


def attend_group(q_heads, k_heads, v_heads, segment, heads_here):
    group_rows = q_heads.shape[0]
    block_rows = min(512, group_rows)
    count_blocks = group_rows // block_rows
    q_blocks = q_heads.reshape(count_blocks, block_rows, heads_here, HD)
    seg_blocks = segment.reshape(count_blocks, block_rows)
    k_split = k_heads.reshape(group_rows, heads_here, HD)
    v_split = v_heads.reshape(group_rows, heads_here, HD)

    def one_block(block_pair):
        q_block, seg_block = block_pair
        scores = jnp.einsum(
            "qhd,khd->hqk", q_block, k_split, preferred_element_type=jnp.float32
        ) / math.sqrt(HD)
        same_prompt = seg_block[:, None] == segment[None, :]
        scores = jnp.where(same_prompt[None, :, :], scores, -jnp.inf)
        row_max = jnp.max(scores, axis=2, keepdims=True)
        weights = jnp.exp(scores - row_max)
        totals = jnp.sum(weights, axis=2)
        output = jnp.einsum(
            "hqk,khd->qhd",
            weights.astype(jnp.bfloat16),
            v_split,
            preferred_element_type=jnp.float32,
        )
        output = output / jnp.transpose(totals)[:, :, None]
        return output.astype(jnp.bfloat16).reshape(block_rows, heads_here * HD)

    return lax.map(one_block, (q_blocks, seg_blocks)).reshape(group_rows, heads_here * HD)


def body(
    residual,
    queries,
    new_keys,
    new_values,
    lengths,
    page_order,
    wo_shard,
    norm_gain,
    gate_shard,
    up_shard,
    down_shard,
    routes,
    route_weights,
):
    tensor_count = lax.axis_size("tensor")
    heads_here = HEADS // tensor_count
    pieces = [wo_shard.T, gate_shard[0], up_shard[0], down_shard[0]]
    packed = jnp.concatenate([p.reshape(-1) for p in pieces]).astype(jnp.bfloat16).reshape(-1, 128)
    pairs = lax.all_gather(packed, "dh")
    pairs, queries, new_keys, new_values = lax.optimization_barrier(
        (pairs, queries, new_keys, new_values)
    )
    q_heads, k_heads, v_heads = (
        lax.all_to_all(queries, "tensor", split_axis=1, concat_axis=0, tiled=True),
        lax.all_to_all(new_keys, "tensor", split_axis=1, concat_axis=0, tiled=True),
        lax.all_to_all(new_values, "tensor", split_axis=1, concat_axis=0, tiled=True),
    )
    group_rows = q_heads.shape[0]
    pool_size = page_order.shape[1]
    segment, slot_index = page_layout(lengths[0], page_order[0], group_rows, pool_size)
    head_width = k_heads.shape[1]
    key_pages = (
        jnp.zeros((pool_size * PAGE, head_width), jnp.bfloat16)
        .at[slot_index]
        .set(k_heads)
        .reshape(pool_size, PAGE, head_width)
    )
    value_pages = (
        jnp.zeros((pool_size * PAGE, head_width), jnp.bfloat16)
        .at[slot_index]
        .set(v_heads)
        .reshape(pool_size, PAGE, head_width)
    )
    gathered = lax.all_gather(pairs, "dz")
    attended = attend_group(q_heads, k_heads, v_heads, segment, heads_here)
    token_rows = lax.all_to_all(attended, "tensor", split_axis=0, concat_axis=1, tiled=True)
    flight = tensor_count // SPLIT
    flight_ids = jnp.arange(flight, dtype=jnp.int32)
    named_here = routes[:, :, None] == flight_ids[None, None, :]
    routed = jnp.any(named_here, axis=1)
    weight_sum = jnp.sum(jnp.where(named_here, route_weights[:, :, None], 0.0), axis=1)
    ranked = jnp.cumsum(routed.astype(jnp.int32), axis=0) - 1
    picked = (ranked[:, :, None] == jnp.arange(MOST, dtype=jnp.int32)[None, None, :]) & routed[
        :, :, None
    ]
    selector = picked.astype(jnp.bfloat16)
    outgoing = jnp.concatenate(
        [
            jnp.einsum("tem,td->emd", selector, token_rows, preferred_element_type=jnp.float32),
            jnp.einsum("tem,td->emd", selector, residual, preferred_element_type=jnp.float32),
        ],
        axis=2,
    ).astype(jnp.bfloat16)
    outgoing = jnp.repeat(outgoing, SPLIT, axis=0)
    arrived = lax.all_to_all(outgoing, "tensor", split_axis=0, concat_axis=0, tiled=True)
    gathered, arrived, token_rows = lax.optimization_barrier((gathered, arrived, token_rows))
    wo_piece_rows = pieces[0].size // 128
    wo_cols = jnp.swapaxes(gathered[:, :, :wo_piece_rows], 0, 1).reshape(-1, pieces[0].shape[1])
    wo_full = lax.all_gather(wo_cols, "tensor", axis=1, tiled=True)
    experts = jnp.swapaxes(gathered[:, :, wo_piece_rows:], 0, 1)
    experts = experts.reshape(experts.shape[0] * experts.shape[1], -1)
    weights_full, at = [], 0
    for p in pieces[1:]:
        weights_full.append(experts[:, at : at + p.size].reshape((-1,) + p.shape))
        at += p.size
    gate_full = weights_full[0].reshape(-1, gate_shard.shape[2])
    up_full = weights_full[1].reshape(-1, up_shard.shape[2])
    down_full = weights_full[2].transpose(1, 0, 2).reshape(down_shard.shape[1], -1)

    arrived, key_pages, value_pages, gate_full, up_full, down_full = lax.optimization_barrier(
        (arrived, key_pages, value_pages, gate_full, up_full, down_full)
    )

    def project_norm(rows_att, rows_res):
        projected = jnp.einsum(
            "...r,cr->...c", rows_att, wo_full, preferred_element_type=jnp.float32
        )
        mid = (rows_res.astype(jnp.float32) + projected).astype(jnp.bfloat16)
        mid_float = mid.astype(jnp.float32)
        normed = (
            mid_float
            * lax.rsqrt(jnp.mean(mid_float * mid_float, axis=-1, keepdims=True) + 1e-06)
            * norm_gain
        ).astype(jnp.bfloat16)
        return mid, normed

    _, arrived_normed = project_norm(arrived[:, :, :D], arrived[:, :, D:])
    gate_val = jnp.einsum("smd,dp->smp", arrived_normed, gate_full, preferred_element_type=jnp.float32)
    up_val = jnp.einsum("smd,dp->smp", arrived_normed, up_full, preferred_element_type=jnp.float32)
    inner_act = (jax.nn.silu(gate_val) * up_val).astype(jnp.bfloat16)
    result = jnp.einsum(
        "smp,pd->smd", inner_act, down_full, preferred_element_type=jnp.float32
    ).astype(jnp.bfloat16)
    returned = lax.all_to_all(result, "tensor", split_axis=0, concat_axis=0, tiled=True)
    hidden_mid, _ = project_norm(token_rows, residual)
    summed = jnp.sum(returned.reshape(flight, SPLIT, MOST, D).astype(jnp.float32), axis=1)
    mixing = picked.astype(jnp.float32) * weight_sum[:, :, None]
    expert_sum = jnp.einsum("tem,emd->td", mixing, summed, precision=lax.Precision.HIGHEST).astype(
        jnp.bfloat16
    )
    return (hidden_mid, expert_sum, key_pages, value_pages)


def solution(mesh):
    dp_count = mesh.shape["dp"]
    dz_count = 16 if dp_count % 16 == 0 else dp_count
    split_mesh = Mesh(
        mesh.devices.reshape(dp_count // dz_count, dz_count, mesh.shape["tensor"]),
        ("dh", "dz", "tensor"),
    )
    return jax.shard_map(
        body,
        mesh=split_mesh,
        in_specs=(
            P(("dh", "dz", "tensor"), None),
            P(("dh", "dz", "tensor"), None),
            P(("dh", "dz", "tensor"), None),
            P(("dh", "dz", "tensor"), None),
            P(("dh", "dz"), None),
            P(("dh", "dz"), None),
            P("tensor", ("dh", "dz")),
            P(),
            P("tensor", ("dh", "dz"), None),
            P("tensor", ("dh", "dz"), None),
            P("tensor", None, ("dh", "dz")),
            P(("dh", "dz", "tensor"), None),
            P(("dh", "dz", "tensor"), None),
        ),
        out_specs=(
            P(("dh", "dz", "tensor"), None),
            P(("dh", "dz", "tensor"), None),
            P(("dh", "dz"), None, "tensor"),
            P(("dh", "dz"), None, "tensor"),
        ),
        check_vma=False,
    )
```

```python
import math

import jax
import jax.numpy as jnp
from jax import lax
from jax.sharding import Mesh, PartitionSpec as P

D = 2048
HEADS = 16
HD = 128
SPLIT = 4
PAGE = 128
MOST = 16


def page_layout(lens_row, order_row, group_rows, pool_size):
    index_rows = jnp.arange(group_rows, dtype=jnp.int32)
    prompt_ends = jnp.cumsum(lens_row)
    segment = jnp.sum((index_rows[:, None] >= prompt_ends[None, :]).astype(jnp.int32), axis=1)
    prompt_starts = prompt_ends - lens_row
    owner_mask = (
        segment[:, None] == jnp.arange(lens_row.shape[0], dtype=jnp.int32)[None, :]
    ).astype(jnp.int32)
    begins = jnp.sum(owner_mask * prompt_starts[None, :], axis=1)
    page_count = (lens_row + PAGE - 1) // PAGE
    first_page = jnp.cumsum(page_count) - page_count
    page_first = jnp.sum(owner_mask * first_page[None, :], axis=1)
    position = index_rows - begins
    logical = page_first + position // PAGE
    matched = (logical[:, None] == jnp.arange(pool_size, dtype=jnp.int32)[None, :]).astype(
        jnp.int32
    )
    physical = jnp.sum(matched * order_row[None, :], axis=1)
    return (segment, physical * PAGE + position % PAGE)


def attend_group(q_heads, k_heads, v_heads, segment, heads_here):
    group_rows = q_heads.shape[0]
    block_rows = min(512, group_rows)
    count_blocks = group_rows // block_rows
    q_blocks = q_heads.reshape(count_blocks, block_rows, heads_here, HD)
    seg_blocks = segment.reshape(count_blocks, block_rows)
    k_split = k_heads.reshape(group_rows, heads_here, HD)
    v_split = v_heads.reshape(group_rows, heads_here, HD)

    def one_block(block_pair):
        q_block, seg_block = block_pair
        scores = jnp.einsum(
            "qhd,khd->hqk", q_block, k_split, preferred_element_type=jnp.float32
        ) / math.sqrt(HD)
        same_prompt = seg_block[:, None] == segment[None, :]
        scores = jnp.where(same_prompt[None, :, :], scores, -jnp.inf)
        row_max = jnp.max(scores, axis=2, keepdims=True)
        weights = jnp.exp(scores - row_max)
        totals = jnp.sum(weights, axis=2)
        output = jnp.einsum(
            "hqk,khd->qhd",
            weights.astype(jnp.bfloat16),
            v_split,
            preferred_element_type=jnp.float32,
        )
        output = output / jnp.transpose(totals)[:, :, None]
        return output.astype(jnp.bfloat16).reshape(block_rows, heads_here * HD)

    return lax.map(one_block, (q_blocks, seg_blocks)).reshape(group_rows, heads_here * HD)


def body(
    residual,
    queries,
    new_keys,
    new_values,
    lengths,
    page_order,
    wo_shard,
    norm_gain,
    gate_shard,
    up_shard,
    down_shard,
    routes,
    route_weights,
):
    tensor_count = lax.axis_size("tensor")
    heads_here = HEADS // tensor_count
    q_heads, k_heads, v_heads = (
        lax.all_to_all(queries, "tensor", split_axis=1, concat_axis=0, tiled=True),
        lax.all_to_all(new_keys, "tensor", split_axis=1, concat_axis=0, tiled=True),
        lax.all_to_all(new_values, "tensor", split_axis=1, concat_axis=0, tiled=True),
    )
    group_rows = q_heads.shape[0]
    pool_size = page_order.shape[1]
    segment, slot_index = page_layout(lengths[0], page_order[0], group_rows, pool_size)
    head_width = k_heads.shape[1]
    key_pages = (
        jnp.zeros((pool_size * PAGE, head_width), jnp.bfloat16)
        .at[slot_index]
        .set(k_heads)
        .reshape(pool_size, PAGE, head_width)
    )
    value_pages = (
        jnp.zeros((pool_size * PAGE, head_width), jnp.bfloat16)
        .at[slot_index]
        .set(v_heads)
        .reshape(pool_size, PAGE, head_width)
    )
    pieces = [wo_shard.T, gate_shard[0], up_shard[0], down_shard[0]]
    packed = jnp.concatenate([p.reshape(-1) for p in pieces]).astype(jnp.bfloat16).reshape(-1, 128)
    gathered = lax.all_gather(lax.all_gather(packed, "dh"), "dz")
    attended = attend_group(q_heads, k_heads, v_heads, segment, heads_here)
    token_rows = lax.all_to_all(attended, "tensor", split_axis=0, concat_axis=1, tiled=True)
    flight = tensor_count // SPLIT
    flight_ids = jnp.arange(flight, dtype=jnp.int32)
    named_here = routes[:, :, None] == flight_ids[None, None, :]
    routed = jnp.any(named_here, axis=1)
    weight_sum = jnp.sum(jnp.where(named_here, route_weights[:, :, None], 0.0), axis=1)
    ranked = jnp.cumsum(routed.astype(jnp.int32), axis=0) - 1
    picked = (ranked[:, :, None] == jnp.arange(MOST, dtype=jnp.int32)[None, None, :]) & routed[
        :, :, None
    ]
    selector = picked.astype(jnp.bfloat16)
    residual_out = jnp.einsum(
        "tem,td->emd", selector, residual, preferred_element_type=jnp.float32
    ).astype(jnp.bfloat16)
    residual_in = lax.all_to_all(
        jnp.repeat(residual_out, SPLIT, axis=0), "tensor", split_axis=0, concat_axis=0, tiled=True
    )
    gathered, token_rows, residual_in = lax.optimization_barrier((gathered, token_rows, residual_in))
    wo_piece_rows = pieces[0].size // 128
    wo_cols = jnp.swapaxes(gathered[:, :, :wo_piece_rows], 0, 1).reshape(-1, pieces[0].shape[1])
    wo_full = lax.all_gather(wo_cols, "tensor", axis=1, tiled=True)
    experts = jnp.swapaxes(gathered[:, :, wo_piece_rows:], 0, 1)
    experts = experts.reshape(experts.shape[0] * experts.shape[1], -1)
    weights_full, at = [], 0
    for p in pieces[1:]:
        weights_full.append(experts[:, at : at + p.size].reshape((-1,) + p.shape))
        at += p.size
    gate_full = weights_full[0].reshape(-1, gate_shard.shape[2])
    up_full = weights_full[1].reshape(-1, up_shard.shape[2])
    down_full = weights_full[2].transpose(1, 0, 2).reshape(down_shard.shape[1], -1)

    outgoing = jnp.einsum(
        "tem,td->emd", selector, token_rows, preferred_element_type=jnp.float32
    ).astype(jnp.bfloat16)
    outgoing = jnp.repeat(outgoing, SPLIT, axis=0)
    outgoing, gate_full, up_full, down_full, key_pages, value_pages = lax.optimization_barrier(
        (outgoing, gate_full, up_full, down_full, key_pages, value_pages)
    )
    arrived = lax.all_to_all(outgoing, "tensor", split_axis=0, concat_axis=0, tiled=True)

    def project_norm(rows_att, rows_res):
        projected = jnp.einsum(
            "...r,cr->...c", rows_att, wo_full, preferred_element_type=jnp.float32
        )
        mid = (rows_res.astype(jnp.float32) + projected).astype(jnp.bfloat16)
        mid_float = mid.astype(jnp.float32)
        normed = (
            mid_float
            * lax.rsqrt(jnp.mean(mid_float * mid_float, axis=-1, keepdims=True) + 1e-06)
            * norm_gain
        ).astype(jnp.bfloat16)
        return mid, normed

    _, arrived_normed = project_norm(arrived, residual_in)
    gate_val = jnp.einsum("smd,dp->smp", arrived_normed, gate_full, preferred_element_type=jnp.float32)
    up_val = jnp.einsum("smd,dp->smp", arrived_normed, up_full, preferred_element_type=jnp.float32)
    inner_act = (jax.nn.silu(gate_val) * up_val).astype(jnp.bfloat16)
    result = jnp.einsum(
        "smp,pd->smd", inner_act, down_full, preferred_element_type=jnp.float32
    ).astype(jnp.bfloat16)
    returned = lax.all_to_all(result, "tensor", split_axis=0, concat_axis=0, tiled=True)
    hidden_mid, _ = project_norm(token_rows, residual)
    summed = jnp.sum(returned.reshape(flight, SPLIT, MOST, D).astype(jnp.float32), axis=1)
    mixing = picked.astype(jnp.float32) * weight_sum[:, :, None]
    expert_sum = jnp.einsum("tem,emd->td", mixing, summed, precision=lax.Precision.HIGHEST).astype(
        jnp.bfloat16
    )
    return (hidden_mid, expert_sum, key_pages, value_pages)


def solution(mesh):
    dp_count = mesh.shape["dp"]
    dz_count = 16 if dp_count % 16 == 0 else dp_count
    split_mesh = Mesh(
        mesh.devices.reshape(dp_count // dz_count, dz_count, mesh.shape["tensor"]),
        ("dh", "dz", "tensor"),
    )
    return jax.shard_map(
        body,
        mesh=split_mesh,
        in_specs=(
            P(("dh", "dz", "tensor"), None),
            P(("dh", "dz", "tensor"), None),
            P(("dh", "dz", "tensor"), None),
            P(("dh", "dz", "tensor"), None),
            P(("dh", "dz"), None),
            P(("dh", "dz"), None),
            P("tensor", ("dh", "dz")),
            P(),
            P("tensor", ("dh", "dz"), None),
            P("tensor", ("dh", "dz"), None),
            P("tensor", None, ("dh", "dz")),
            P(("dh", "dz", "tensor"), None),
            P(("dh", "dz", "tensor"), None),
        ),
        out_specs=(
            P(("dh", "dz", "tensor"), None),
            P(("dh", "dz", "tensor"), None),
            P(("dh", "dz"), None, "tensor"),
            P(("dh", "dz"), None, "tensor"),
        ),
        check_vma=False,
    )
```
